256 devices in a mesh: blk: 8 (over y_lo, x), wide: 32 (over y_hi, z, core).
Axes of the slice: x: 4, y: 4 (y_hi: 2, y_lo: 2; y = y_hi * 2 + y_lo), z: 8, core: 2. Of those that a mesh axis runs over, the one named last changes fastest.
Arguments:
- a_blocks: float32 [32, 8, 32, 4, 128, 128], P('blk', None, 'wide'), may hold values from -6 to 6
- a_map: int32 [32, 8, 32, 4], P('blk', None, 'wide'), may hold values 0 or 1
- b_blocks: float32 [8, 32, 4, 8, 128, 128], P('blk', 'wide'), may hold values from -0.03125 to 0.03125
- b_map: int32 [8, 32, 4, 8], P('blk', 'wide'), may hold values 0 or 1
- owner_map: int32 [32, 8], P('blk'), may hold values from -1 to 31, as said below
Outputs:
- owned: float32 [8, 32, 2, 128, 128], P('blk', 'wide')
The draws below stay inside these ranges and needn't reach their ends.
Inputs may be any that keep to these rules, and one draw needn't show every extreme that they name: `owner_map`: in each panel of 4 x 8 product blocks (block rows i * 4 to i * 4 + 3), each owner holds at most 2 blocks, and one owner holds exactly 2.
All inputs are finite; a program needn't handle non-finite values. No bound on the sum of `a_map` or of `b_map` on one device may be relied on, other than what follows from the above.
Results may differ from the reference program's by a relative error of at most 0.00007.
Values sent between devices are 32-bit elements; how exact they have to be, the bound alone decides.
No kernel may reach another device: no remote copies, remote signals or barrier semaphores. Data moves between devices by JAX's collectives and lax.ppermute only.
A program may use at most 128 MiB of HBM per device.

```python
import jax
import jax.numpy as jnp
from jax import lax

BS = 128
KBD = 4
RB = 4
CBT = 8
NRB = 32
ORDER = 131072
CAP = 2
N_BLK = 8
N_WIDE = 32


def draw_owner_map(key, part):
    panel_size = RB * CBT
    pool_size = (N_WIDE - 1) * CAP + panel_size // 4

    def one_panel(panel_key):
        first_key, second_key, third_key = jax.random.split(panel_key, 3)
        busiest = jax.random.randint(first_key, (), 0, N_WIDE, dtype=jnp.int32)
        places = jnp.arange(pool_size, dtype=jnp.int32)
        others = (busiest + 1 + places // CAP) % N_WIDE
        pool = jnp.where(places < (N_WIDE - 1) * CAP, others, -1).astype(jnp.int32)
        pool = jax.random.permutation(second_key, pool)
        listed = jnp.concatenate([jnp.zeros((CAP,), jnp.int32) + busiest, pool[:panel_size - CAP]])
        listed = jax.random.permutation(third_key, listed)
        return listed.reshape(RB, CBT)
    panel_keys = jax.random.split(jax.random.fold_in(key, 17), N_BLK)
    return jax.vmap(one_panel)(panel_keys).reshape(N_BLK * RB, CBT).astype(jnp.int32)


def plant(array, own_key, low, largest):
    extent = array.shape
    spot = [jax.random.randint(jax.random.fold_in(own_key, axis), (), 0, extent[axis]) for axis in range(len(extent))]
    array = array.at[tuple(spot)].set(low)
    longest = extent.index(max(extent))
    spot[longest] = (spot[longest] + 1) % extent[longest]
    return array.at[tuple(spot)].set(largest)


def block_scale(key, shape, pieces, least, high):
    def one(axis_at, parts):
        draws = jax.random.uniform(jax.random.fold_in(jax.random.fold_in(key, 6), axis_at), (parts,), jnp.float32, least / len(pieces), high / len(pieces))
        return jnp.repeat(jnp.exp(draws), shape[axis_at] // parts).reshape((-1,) + (1,) * (len(shape) - axis_at - 1))

    level = one(*pieces[0])
    for cut in pieces[1:]:
        level = level * one(*cut)
    return level


def scatter_about(own_key, dims, spread, most, shards=(), kind=jnp.bfloat16):
    loudness = block_scale(own_key, dims, shards, -0.22, 0.18) if shards else 1.0
    array = jax.random.normal(own_key, dims, jnp.float32) * spread * loudness
    return jnp.minimum(jnp.maximum(array, -most), most).astype(kind)


def setup_inputs(seed: int = 0) -> dict:
    seeds = jax.random.split(jax.random.key(seed), 6)
    return {
        "a_blocks": scatter_about(seeds[0], (NRB, N_BLK, N_WIDE, KBD, BS, BS), 1.0, 6.0, ((0, 8), (2, 32)), jnp.float32),
        "a_map": plant((jax.random.randint(seeds[1], (NRB, N_BLK, N_WIDE, KBD), 0, 2) < 1).astype(jnp.int32), jax.random.fold_in(seeds[1], 1), 0, 1),
        "b_blocks": scatter_about(seeds[2], (N_BLK, N_WIDE, KBD, CBT, BS, BS), (ORDER // 4) ** -0.5, 0.03125, ((0, 8), (1, 32)), jnp.float32),
        "b_map": plant((jax.random.randint(seeds[3], (N_BLK, N_WIDE, KBD, CBT), 0, 2) < 1).astype(jnp.int32), jax.random.fold_in(seeds[3], 1), 0, 1),
        "owner_map": draw_owner_map(jax.random.fold_in(seeds[5], 71), 0),
    }


def reference(a_blocks, a_map, b_blocks, b_map, owner_map):
    highest = lax.Precision.HIGHEST
    right_used = b_blocks * b_map[..., None, None].astype(b_blocks.dtype)

    def one_row(row_pair):
        block_row, row_mask = row_pair
        left_used = block_row * row_mask[..., None, None].astype(block_row.dtype)
        return jnp.einsum("jwtxy,jwtcyz->cxz", left_used, right_used, precision=highest)

    product = lax.map(one_row, (a_blocks, a_map))
    groups = product.reshape(N_BLK, RB * CBT, BS, BS)
    owner_list = owner_map.reshape(N_BLK, RB * CBT)
    owner_hit = (owner_list[:, :, None] == jnp.arange(N_WIDE, dtype=jnp.int32)[None, None, :]).astype(jnp.int32)
    slot_rank = jnp.cumsum(owner_hit, axis=1) - owner_hit
    slot_match = (slot_rank[..., None] == jnp.arange(CAP, dtype=jnp.int32)).astype(jnp.int32)
    selector = (owner_hit[..., None] * slot_match).astype(product.dtype)
    return jnp.einsum("iqos,iqxy->iosxy", selector, groups, precision=highest)
```

```python
import jax
import jax.numpy as jnp
from jax import lax
from jax.sharding import PartitionSpec as P


def moved(value, axis, target):
    devices = lax.axis_size(axis)
    return lax.ppermute(value, axis, [(i, target(i)) for i in range(devices)])


def per_device(a_blocks, a_map, b_blocks, b_map, owner_map, row_len):
    highest = lax.Precision.HIGHEST
    cycle_size = lax.axis_size("blk")
    wide_size = lax.axis_size("wide")
    n_rows = cycle_size // row_len
    myself = lax.axis_index("blk")
    me_wide = lax.axis_index("wide")
    row = myself // row_len
    col = myself % row_len
    other_row = (row + 1) % n_rows

    def right(i):
        return (i // row_len) * row_len + (i % row_len + 1) % row_len

    def left(i):
        return (i // row_len) * row_len + (i % row_len - 1) % row_len

    def partner(i):
        return (i + row_len) % cycle_size

    left_used = a_blocks[:, :, 0] * a_map[:, :, 0, :, None, None].astype(jnp.float32)
    right_used = b_blocks[0, 0] * b_map[0, 0][:, :, None, None].astype(jnp.float32)
    rows_here, cols_here = owner_map.shape
    block_side = right_used.shape[-1]
    half = cols_here // 2

    partner_left = {}
    for offset in (0, 1, row_len - 1, 2):
        sent = lax.dynamic_index_in_dim(
            left_used, other_row * row_len + (col + offset) % row_len, 1, keepdims=False
        )
        partner_left[offset] = moved(sent, "blk", partner)

    partner_owners = moved(owner_map, "blk", partner)

    from_right = moved(right_used, "blk", left)
    from_left = moved(right_used, "blk", right)
    far_low = moved(from_left[:, :half], "blk", right)
    far_high = moved(from_right[:, half:], "blk", left)

    def left_pair(offset):
        k = (col + offset) % row_len
        own = lax.dynamic_index_in_dim(left_used, row * row_len + k, 1, keepdims=False)
        return jnp.concatenate([own, partner_left[offset]], axis=0)

    def product(lhs, rhs):
        return jnp.einsum("rtxy,tcyz->rcxz", lhs, rhs, precision=highest)

    partial_value = product(left_pair(0), right_used)
    partial_value = partial_value + product(left_pair(1), from_right)
    partial_value = partial_value + product(left_pair(row_len - 1), from_left)
    far = left_pair(2)
    partial_value = partial_value + jnp.concatenate(
        [product(far, far_low), product(far, far_high)], axis=1
    )

    block_count = rows_here * cols_here
    stacked = partial_value.reshape(2, block_count, block_side, block_side)
    summed = lax.psum(stacked, "wide")

    def owned_slots(owner_list, panel):
        owner_hit = (owner_list == me_wide).astype(jnp.int32)
        slot_rank = jnp.cumsum(owner_hit) - owner_hit
        slots = []
        for slot in range(2):
            chosen = (owner_hit == 1) & (slot_rank == slot)
            index = jnp.argmax(chosen)
            taken = jnp.any(chosen)
            block = lax.dynamic_index_in_dim(panel, index, 0, keepdims=False)
            slots.append(jnp.where(taken, block, jnp.zeros_like(block)))
        return jnp.stack(slots)

    mine = owned_slots(owner_map.reshape(block_count), summed[0])
    for_partner = owned_slots(partner_owners.reshape(block_count), summed[1])
    slots = mine + moved(for_partner, "blk", partner)
    return slots[None, None]


def solution(mesh):
    in_specs = (
        P("blk", None, "wide", None, None, None),
        P("blk", None, "wide", None),
        P("blk", "wide", None, None, None, None),
        P("blk", "wide", None, None),
        P("blk", None),
    )
    out_specs = P("blk", "wide", None, None, None)
    row_len = 4

    def body(*args):
        return per_device(*args, row_len=row_len)

    return jax.shard_map(
        body, mesh=mesh, in_specs=in_specs, out_specs=out_specs, check_vma=False
    )
```

```python
import jax
import jax.numpy as jnp
from jax import lax
from jax.sharding import PartitionSpec as P


def moved(value, axis, target):
    devices = lax.axis_size(axis)
    return lax.ppermute(value, axis, [(i, target(i)) for i in range(devices)])


def per_device(a_blocks, a_map, b_blocks, b_map, owner_map, row_len, wide_layout):
    highest = lax.Precision.HIGHEST
    cycle_size = lax.axis_size("blk")
    wide_size = lax.axis_size("wide")
    n_rows = cycle_size // row_len
    myself = lax.axis_index("blk")
    me_wide = lax.axis_index("wide")
    row = myself // row_len
    col = myself % row_len
    other_row = (row + 1) % n_rows

    def right(i):
        return (i // row_len) * row_len + (i % row_len + 1) % row_len

    def left(i):
        return (i // row_len) * row_len + (i % row_len - 1) % row_len

    def partner(i):
        return (i + row_len) % cycle_size

    left_used = a_blocks[:, :, 0] * a_map[:, :, 0, :, None, None].astype(jnp.float32)
    right_used = b_blocks[0, 0] * b_map[0, 0][:, :, None, None].astype(jnp.float32)
    rows_here, cols_here = owner_map.shape
    block_side = right_used.shape[-1]
    half = cols_here // 2

    partner_left = {}
    for offset in (0, 1, row_len - 1, 2):
        sent = lax.dynamic_index_in_dim(
            left_used, other_row * row_len + (col + offset) % row_len, 1, keepdims=False
        )
        partner_left[offset] = moved(sent, "blk", partner)

    partner_owners = moved(owner_map, "blk", partner)

    from_right = moved(right_used, "blk", left)
    from_left = moved(right_used, "blk", right)
    far_low = moved(from_left[:, :half], "blk", right)
    far_high = moved(from_right[:, half:], "blk", left)

    def left_pair(offset):
        k = (col + offset) % row_len
        own = lax.dynamic_index_in_dim(left_used, row * row_len + k, 1, keepdims=False)
        return jnp.concatenate([own, partner_left[offset]], axis=0)

    def product(lhs, rhs):
        return jnp.einsum("rtxy,tcyz->rcxz", lhs, rhs, precision=highest)

    partial_value = product(left_pair(0), right_used)
    partial_value = partial_value + product(left_pair(1), from_right)
    partial_value = partial_value + product(left_pair(row_len - 1), from_left)
    far = left_pair(2)
    partial_value = partial_value + jnp.concatenate(
        [product(far, far_low), product(far, far_high)], axis=1
    )

    block_count = rows_here * cols_here
    stacked = partial_value.reshape(2, block_count, block_side, block_side)
    slots_each = 2

    def selector(owner_list):
        owner_hit = (owner_list[:, None] == jnp.arange(wide_size, dtype=jnp.int32)[None, :]).astype(
            jnp.int32
        )
        slot_rank = jnp.cumsum(owner_hit, axis=0) - owner_hit
        slot_match = (slot_rank[:, :, None] == jnp.arange(slots_each, dtype=jnp.int32)).astype(
            jnp.int32
        )
        return (owner_hit[:, :, None] * slot_match).astype(jnp.float32)

    chooser = jnp.stack(
        [selector(owner_map.reshape(block_count)), selector(partner_owners.reshape(block_count))]
    )
    slotted = jnp.einsum("pqos,pqxy->posxy", chooser, stacked, precision=highest)
    n_hi, n_z, n_core = wide_layout
    hi = me_wide // (n_z * n_core)
    zi = (me_wide // n_core) % n_z
    ci = me_wide % n_core

    def wide_of(h, z, c):
        return (h * n_z + z) * n_core + c

    def sibling(w):
        return wide_of(w // (n_z * n_core), (w // n_core) % n_z, (w % n_core + 1) % n_core)

    def z_next(w):
        return wide_of(w // (n_z * n_core), ((w // n_core) % n_z + 1) % n_z, w % n_core)

    def z_prev(w):
        return wide_of(w // (n_z * n_core), ((w // n_core) % n_z - 1) % n_z, w % n_core)

    def hi_partner(w):
        return wide_of((w // (n_z * n_core) + 1) % n_hi, (w // n_core) % n_z, w % n_core)

    slotted = slotted.reshape(2, n_hi, n_z, n_core, slots_each, block_side, block_side)
    kept = lax.dynamic_index_in_dim(slotted, ci, 3, keepdims=False)
    given = lax.dynamic_index_in_dim(slotted, (ci + 1) % n_core, 3, keepdims=False)
    acc = kept + moved(given, "wide", sibling)
    ahead = acc[:, :, :, 0]
    behind = acc[:, :, :, 1]

    def chunk(value, index):
        return lax.dynamic_index_in_dim(value, index % n_z, 2, keepdims=False)

    sent_ahead = chunk(ahead, zi - 1)
    sent_behind = chunk(behind, zi + 1)
    for step in range(n_z - 1):
        got_ahead = moved(sent_ahead, "wide", z_next)
        got_behind = moved(sent_behind, "wide", z_prev)
        if step + 1 < n_z - 1:
            sent_ahead = got_ahead + chunk(ahead, zi - 2 - step)
            sent_behind = got_behind + chunk(behind, zi + 2 + step)
    done_z = jnp.stack(
        [got_ahead + chunk(ahead, zi), got_behind + chunk(behind, zi)], axis=2
    )
    kept = lax.dynamic_index_in_dim(done_z, hi, 1, keepdims=False)
    given = lax.dynamic_index_in_dim(done_z, (hi + 1) % n_hi, 1, keepdims=False)
    reduced = kept + moved(given, "wide", hi_partner)
    slots = reduced[0] + moved(reduced[1], "blk", partner)
    return slots[None, None]


def solution(mesh):
    in_specs = (
        P("blk", None, "wide", None, None, None),
        P("blk", None, "wide", None),
        P("blk", "wide", None, None, None, None),
        P("blk", "wide", None, None),
        P("blk", None),
    )
    out_specs = P("blk", "wide", None, None, None)
    row_len = 4
    wide_layout = (2, 8, 2)

    def body(*args):
        return per_device(*args, row_len=row_len, wide_layout=wide_layout)

    return jax.shard_map(
        body, mesh=mesh, in_specs=in_specs, out_specs=out_specs, check_vma=False
    )
```

```python
import jax
import jax.numpy as jnp
from jax import lax
from jax.sharding import PartitionSpec as P


def moved(value, axis, target):
    devices = lax.axis_size(axis)
    return lax.ppermute(value, axis, [(i, target(i)) for i in range(devices)])


def per_device(a_blocks, a_map, b_blocks, b_map, owner_map, row_len, wide_layout):
    highest = lax.Precision.HIGHEST
    cycle_size = lax.axis_size("blk")
    wide_size = lax.axis_size("wide")
    n_rows = cycle_size // row_len
    myself = lax.axis_index("blk")
    me_wide = lax.axis_index("wide")
    row = myself // row_len
    col = myself % row_len
    other_row = (row + 1) % n_rows

    def right(i):
        return (i // row_len) * row_len + (i % row_len + 1) % row_len

    def left(i):
        return (i // row_len) * row_len + (i % row_len - 1) % row_len

    def partner(i):
        return (i + row_len) % cycle_size

    left_used = a_blocks[:, :, 0] * a_map[:, :, 0, :, None, None].astype(jnp.float32)
    right_used = b_blocks[0, 0] * b_map[0, 0][:, :, None, None].astype(jnp.float32)
    rows_here, cols_here = owner_map.shape
    block_side = right_used.shape[-1]
    half = cols_here // 2

    partner_left = {}
    for offset in (0, 1, row_len - 1, 2):
        sent = lax.dynamic_index_in_dim(
            left_used, other_row * row_len + (col + offset) % row_len, 1, keepdims=False
        )
        partner_left[offset] = moved(sent, "blk", partner)

    partner_owners = moved(owner_map, "blk", partner)

    from_right = moved(right_used, "blk", left)
    from_left = moved(right_used, "blk", right)
    far_low = moved(from_left[:, :half], "blk", right)
    far_high = moved(from_right[:, half:], "blk", left)

    def own_left(offset):
        k = (col + offset) % row_len
        return lax.dynamic_index_in_dim(left_used, row * row_len + k, 1, keepdims=False)

    def product(lhs, rhs):
        return jnp.einsum("rtxy,tcyz->rcxz", lhs, rhs, precision=highest)

    def panel_partial(left_of):
        total = product(left_of(0), right_used)
        total = total + product(left_of(1), from_right)
        total = total + product(left_of(row_len - 1), from_left)
        far = left_of(2)
        return total + jnp.concatenate([product(far, far_low), product(far, far_high)], axis=1)

    own_partial = panel_partial(own_left)
    partner_partial = panel_partial(lambda offset: partner_left[offset])

    slots_each = 2
    n_hi, n_z, n_core = wide_layout
    hi = me_wide // (n_z * n_core)
    zi = (me_wide // n_core) % n_z
    ci = me_wide % n_core

    def wide_of(h, z, c):
        return (h * n_z + z) * n_core + c

    def sibling(w):
        return wide_of(w // (n_z * n_core), (w // n_core) % n_z, (w % n_core + 1) % n_core)

    def z_next(w):
        return wide_of(w // (n_z * n_core), ((w // n_core) % n_z + 1) % n_z, w % n_core)

    def z_prev(w):
        return wide_of(w // (n_z * n_core), ((w // n_core) % n_z - 1) % n_z, w % n_core)

    def hi_partner(w):
        return wide_of((w // (n_z * n_core) + 1) % n_hi, (w // n_core) % n_z, w % n_core)

    def owner_slots(owner_list, partial, core):
        owners = wide_of(
            jnp.arange(n_hi)[:, None], jnp.arange(n_z)[None, :], core
        ).astype(jnp.int32)
        owner_hit = (owner_list[:, None, None] == owners[None]).astype(jnp.int32)
        slot_rank = jnp.cumsum(owner_hit, axis=0) - owner_hit
        match = (owner_hit[..., None] == 1) & (
            slot_rank[..., None] == jnp.arange(slots_each, dtype=jnp.int32)
        )
        index = jnp.argmax(match, axis=0)
        taken = jnp.any(match, axis=0)
        blocks = partial[index // cols_here, index % cols_here]
        return jnp.where(taken[..., None, None], blocks, jnp.zeros_like(blocks))

    def chunk(value, index):
        return lax.dynamic_index_in_dim(value, index % n_z, 1, keepdims=False)

    def reduce_to_owner(owner_list, partial):
        kept = owner_slots(owner_list, partial, ci)
        given = owner_slots(owner_list, partial, (ci + 1) % n_core)
        acc = kept + moved(given, "wide", sibling)
        ahead = acc[:, :, 0]
        behind = acc[:, :, 1]
        sent_ahead = chunk(ahead, zi - 1)
        sent_behind = chunk(behind, zi + 1)
        for step in range(n_z - 1):
            got_ahead = moved(sent_ahead, "wide", z_next)
            got_behind = moved(sent_behind, "wide", z_prev)
            if step + 1 < n_z - 1:
                sent_ahead = got_ahead + chunk(ahead, zi - 2 - step)
                sent_behind = got_behind + chunk(behind, zi + 2 + step)
        done_z = jnp.stack([got_ahead + chunk(ahead, zi), got_behind + chunk(behind, zi)], axis=1)
        kept = lax.dynamic_index_in_dim(done_z, hi, 0, keepdims=False)
        given = lax.dynamic_index_in_dim(done_z, (hi + 1) % n_hi, 0, keepdims=False)
        return kept + moved(given, "wide", hi_partner)

    block_count = rows_here * cols_here
    mine = reduce_to_owner(owner_map.reshape(block_count), own_partial)
    for_partner = reduce_to_owner(partner_owners.reshape(block_count), partner_partial)
    slots = mine + moved(for_partner, "blk", partner)
    return slots[None, None]


def solution(mesh):
    in_specs = (
        P("blk", None, "wide", None, None, None),
        P("blk", None, "wide", None),
        P("blk", "wide", None, None, None, None),
        P("blk", "wide", None, None),
        P("blk", None),
    )
    out_specs = P("blk", "wide", None, None, None)
    row_len = 4
    wide_layout = (2, 8, 2)

    def body(*args):
        return per_device(*args, row_len=row_len, wide_layout=wide_layout)

    return jax.shard_map(
        body, mesh=mesh, in_specs=in_specs, out_specs=out_specs, check_vma=False
    )
```

```python
import jax
import jax.numpy as jnp
from jax import lax
from jax.sharding import PartitionSpec as P


def moved(value, axis, target):
    devices = lax.axis_size(axis)
    return lax.ppermute(value, axis, [(i, target(i)) for i in range(devices)])


def per_device(a_blocks, a_map, b_blocks, b_map, owner_map, row_len, wide_layout):
    highest = lax.Precision.HIGHEST
    cycle_size = lax.axis_size("blk")
    wide_size = lax.axis_size("wide")
    n_rows = cycle_size // row_len
    myself = lax.axis_index("blk")
    me_wide = lax.axis_index("wide")
    row = myself // row_len
    col = myself % row_len
    other_row = (row + 1) % n_rows

    def right(i):
        return (i // row_len) * row_len + (i % row_len + 1) % row_len

    def left(i):
        return (i // row_len) * row_len + (i % row_len - 1) % row_len

    def partner(i):
        return (i + row_len) % cycle_size

    left_used = a_blocks[:, :, 0] * a_map[:, :, 0, :, None, None].astype(jnp.float32)
    right_used = b_blocks[0, 0] * b_map[0, 0][:, :, None, None].astype(jnp.float32)
    rows_here, cols_here = owner_map.shape
    block_side = right_used.shape[-1]
    half = cols_here // 2

    partner_left = {}
    for offset in (0, 1, row_len - 1, 2):
        sent = lax.dynamic_index_in_dim(
            left_used, other_row * row_len + (col + offset) % row_len, 1, keepdims=False
        )
        partner_left[offset] = moved(sent, "blk", partner)

    partner_owners = moved(owner_map, "blk", partner)

    from_right = moved(right_used, "blk", left)
    from_left = moved(right_used, "blk", right)
    far_low = moved(from_left[:, :half], "blk", right)
    far_high = moved(from_right[:, half:], "blk", left)

    def left_pair(offset):
        k = (col + offset) % row_len
        own = lax.dynamic_index_in_dim(left_used, row * row_len + k, 1, keepdims=False)
        return jnp.concatenate([own, partner_left[offset]], axis=0)

    def product(lhs, rhs):
        return jnp.einsum("rtxy,tcyz->rcxz", lhs, rhs, precision=highest)

    partial_value = product(left_pair(0), right_used)
    partial_value = partial_value + product(left_pair(1), from_right)
    partial_value = partial_value + product(left_pair(row_len - 1), from_left)
    far = left_pair(2)
    partial_value = partial_value + jnp.concatenate(
        [product(far, far_low), product(far, far_high)], axis=1
    )

    n_hi, n_z, n_core = wide_layout
    hi = me_wide // (n_z * n_core)
    zi = (me_wide // n_core) % n_z
    ci = me_wide % n_core

    def wide_of(h, z, c):
        return (h * n_z + z) * n_core + c

    def sibling(w):
        return wide_of(w // (n_z * n_core), (w // n_core) % n_z, (w % n_core + 1) % n_core)

    def z_next(w):
        return wide_of(w // (n_z * n_core), ((w // n_core) % n_z + 1) % n_z, w % n_core)

    def z_prev(w):
        return wide_of(w // (n_z * n_core), ((w // n_core) % n_z - 1) % n_z, w % n_core)

    def hi_partner(w):
        return wide_of((w // (n_z * n_core) + 1) % n_hi, (w // n_core) % n_z, w % n_core)

    partial_value = partial_value + moved(partial_value, "wide", sibling)
    block_count = rows_here * cols_here
    stacked = partial_value.reshape(2, block_count, block_side, block_side)
    slots_each = 2
    owners = wide_of(jnp.arange(n_hi)[:, None], jnp.arange(n_z)[None, :], ci).astype(jnp.int32)

    def selector(owner_list):
        owner_hit = (owner_list[:, None, None] == owners[None]).astype(jnp.int32)
        slot_rank = jnp.cumsum(owner_hit, axis=0) - owner_hit
        slot_match = (slot_rank[..., None] == jnp.arange(slots_each, dtype=jnp.int32)).astype(
            jnp.int32
        )
        return (owner_hit[..., None] * slot_match).astype(jnp.float32)

    chooser = jnp.stack(
        [selector(owner_map.reshape(block_count)), selector(partner_owners.reshape(block_count))]
    )
    acc = jnp.einsum("pqhzs,pqxy->phzsxy", chooser, stacked, precision=highest)
    ahead = acc[:, :, :, 0]
    behind = acc[:, :, :, 1]

    def chunk(value, index):
        return lax.dynamic_index_in_dim(value, index % n_z, 2, keepdims=False)

    sent_ahead = chunk(ahead, zi - 1)
    sent_behind = chunk(behind, zi + 1)
    for step in range(n_z - 1):
        got_ahead = moved(sent_ahead, "wide", z_next)
        got_behind = moved(sent_behind, "wide", z_prev)
        if step + 1 < n_z - 1:
            sent_ahead = got_ahead + chunk(ahead, zi - 2 - step)
            sent_behind = got_behind + chunk(behind, zi + 2 + step)
    done_z = jnp.stack(
        [got_ahead + chunk(ahead, zi), got_behind + chunk(behind, zi)], axis=2
    )
    kept = lax.dynamic_index_in_dim(done_z, hi, 1, keepdims=False)
    given = lax.dynamic_index_in_dim(done_z, (hi + 1) % n_hi, 1, keepdims=False)
    reduced = kept + moved(given, "wide", hi_partner)
    slots = reduced[0] + moved(reduced[1], "blk", partner)
    return slots[None, None]


def solution(mesh):
    in_specs = (
        P("blk", None, "wide", None, None, None),
        P("blk", None, "wide", None),
        P("blk", "wide", None, None, None, None),
        P("blk", "wide", None, None),
        P("blk", None),
    )
    out_specs = P("blk", "wide", None, None, None)
    row_len = 4
    wide_layout = (2, 8, 2)

    def body(*args):
        return per_device(*args, row_len=row_len, wide_layout=wide_layout)

    return jax.shard_map(
        body, mesh=mesh, in_specs=in_specs, out_specs=out_specs, check_vma=False
    )
```

```python
import jax
import jax.numpy as jnp
from jax import lax
from jax.sharding import PartitionSpec as P


def moved(value, axis, target):
    devices = lax.axis_size(axis)
    return lax.ppermute(value, axis, [(i, target(i)) for i in range(devices)])


def per_device(a_blocks, a_map, b_blocks, b_map, owner_map, row_len, wide_layout):
    highest = lax.Precision.HIGHEST
    cycle_size = lax.axis_size("blk")
    wide_size = lax.axis_size("wide")
    n_rows = cycle_size // row_len
    myself = lax.axis_index("blk")
    me_wide = lax.axis_index("wide")
    row = myself // row_len
    col = myself % row_len
    other_row = (row + 1) % n_rows

    def right(i):
        return (i // row_len) * row_len + (i % row_len + 1) % row_len

    def left(i):
        return (i // row_len) * row_len + (i % row_len - 1) % row_len

    def partner(i):
        return (i + row_len) % cycle_size

    left_used = a_blocks[:, :, 0] * a_map[:, :, 0, :, None, None].astype(jnp.float32)
    right_used = b_blocks[0, 0] * b_map[0, 0][:, :, None, None].astype(jnp.float32)
    rows_here, cols_here = owner_map.shape
    block_side = right_used.shape[-1]
    half = cols_here // 2

    partner_left = {}
    for offset in (0, 1, row_len - 1, 2):
        sent = lax.dynamic_index_in_dim(
            left_used, other_row * row_len + (col + offset) % row_len, 1, keepdims=False
        )
        partner_left[offset] = moved(sent, "blk", partner)

    partner_owners = moved(owner_map, "blk", partner)

    from_right = moved(right_used, "blk", left)
    from_left = moved(right_used, "blk", right)
    far_low = moved(from_left[:, :half], "blk", right)
    far_high = moved(from_right[:, half:], "blk", left)

    def left_pair(offset):
        k = (col + offset) % row_len
        own = lax.dynamic_index_in_dim(left_used, row * row_len + k, 1, keepdims=False)
        return jnp.concatenate([own, partner_left[offset]], axis=0)

    def product(lhs, rhs):
        return jnp.einsum("rtxy,tcyz->rcxz", lhs, rhs, precision=highest)

    partial_value = product(left_pair(0), right_used)
    partial_value = partial_value + product(left_pair(1), from_right)
    partial_value = partial_value + product(left_pair(row_len - 1), from_left)
    far = left_pair(2)
    partial_value = partial_value + jnp.concatenate(
        [product(far, far_low), product(far, far_high)], axis=1
    )

    n_hi, n_z, n_core = wide_layout
    hi = me_wide // (n_z * n_core)
    zi = (me_wide // n_core) % n_z
    ci = me_wide % n_core

    def wide_of(h, z, c):
        return (h * n_z + z) * n_core + c

    def sibling(w):
        return wide_of(w // (n_z * n_core), (w // n_core) % n_z, (w % n_core + 1) % n_core)

    def z_next(w):
        return wide_of(w // (n_z * n_core), ((w // n_core) % n_z + 1) % n_z, w % n_core)

    def z_prev(w):
        return wide_of(w // (n_z * n_core), ((w // n_core) % n_z - 1) % n_z, w % n_core)

    def hi_partner(w):
        return wide_of((w // (n_z * n_core) + 1) % n_hi, (w // n_core) % n_z, w % n_core)

    partial_value = partial_value + moved(partial_value, "wide", sibling)
    block_count = rows_here * cols_here
    stacked = partial_value.reshape(2, block_count, block_side, block_side)
    slots_each = 2
    owners = wide_of(jnp.arange(n_hi)[:, None], jnp.arange(n_z)[None, :], ci).astype(jnp.int32)

    def selector(owner_list):
        owner_hit = (owner_list[:, None, None] == owners[None]).astype(jnp.int32)
        slot_rank = jnp.cumsum(owner_hit, axis=0) - owner_hit
        slot_match = (slot_rank[..., None] == jnp.arange(slots_each, dtype=jnp.int32)).astype(
            jnp.int32
        )
        return (owner_hit[..., None] * slot_match).astype(jnp.float32)

    chooser = jnp.stack(
        [selector(owner_map.reshape(block_count)), selector(partner_owners.reshape(block_count))]
    )
    acc = jnp.einsum("pqhzs,pqxy->phzsxy", chooser, stacked, precision=highest)
    def chunk(value, index):
        return lax.dynamic_index_in_dim(value, index % n_z, 2, keepdims=False)

    forward_steps = (n_z - 1) // 2
    backward_steps = n_z - 1 - forward_steps
    sent_ahead = chunk(acc, zi + forward_steps)
    for step in range(forward_steps):
        got_ahead = moved(sent_ahead, "wide", z_next)
        if step + 1 < forward_steps:
            sent_ahead = got_ahead + chunk(acc, zi + forward_steps - step - 1)
    sent_behind = chunk(acc, zi - backward_steps)
    for step in range(backward_steps):
        got_behind = moved(sent_behind, "wide", z_prev)
        if step + 1 < backward_steps:
            sent_behind = got_behind + chunk(acc, zi - backward_steps + step + 1)
    done_z = chunk(acc, zi) + got_ahead + got_behind
    kept = lax.dynamic_index_in_dim(done_z, hi, 1, keepdims=False)
    given = lax.dynamic_index_in_dim(done_z, (hi + 1) % n_hi, 1, keepdims=False)
    reduced = kept + moved(given, "wide", hi_partner)
    slots = reduced[0] + moved(reduced[1], "blk", partner)
    return slots[None, None]


def solution(mesh):
    in_specs = (
        P("blk", None, "wide", None, None, None),
        P("blk", None, "wide", None),
        P("blk", "wide", None, None, None, None),
        P("blk", "wide", None, None),
        P("blk", None),
    )
    out_specs = P("blk", "wide", None, None, None)
    row_len = 4
    wide_layout = (2, 8, 2)

    def body(*args):
        return per_device(*args, row_len=row_len, wide_layout=wide_layout)

    return jax.shard_map(
        body, mesh=mesh, in_specs=in_specs, out_specs=out_specs, check_vma=False
    )
```

```python
import jax
import jax.numpy as jnp
from jax import lax
from jax.sharding import PartitionSpec as P


def moved(value, axis, target):
    devices = lax.axis_size(axis)
    return lax.ppermute(value, axis, [(i, target(i)) for i in range(devices)])


def per_device(a_blocks, a_map, b_blocks, b_map, owner_map, row_len, wide_layout):
    highest = lax.Precision.HIGHEST
    cycle_size = lax.axis_size("blk")
    wide_size = lax.axis_size("wide")
    n_rows = cycle_size // row_len
    myself = lax.axis_index("blk")
    me_wide = lax.axis_index("wide")
    row = myself // row_len
    col = myself % row_len
    other_row = (row + 1) % n_rows

    def right(i):
        return (i // row_len) * row_len + (i % row_len + 1) % row_len

    def left(i):
        return (i // row_len) * row_len + (i % row_len - 1) % row_len

    def partner(i):
        return (i + row_len) % cycle_size

    left_used = a_blocks[:, :, 0] * a_map[:, :, 0, :, None, None].astype(jnp.float32)
    right_used = b_blocks[0, 0] * b_map[0, 0][:, :, None, None].astype(jnp.float32)
    rows_here, cols_here = owner_map.shape
    block_side = right_used.shape[-1]
    half = cols_here // 2

    partner_left = {}
    for offset in (0, 1, row_len - 1, 2):
        sent = lax.dynamic_index_in_dim(
            left_used, other_row * row_len + (col + offset) % row_len, 1, keepdims=False
        )
        partner_left[offset] = moved(sent, "blk", partner)

    partner_owners = moved(owner_map, "blk", partner)

    from_right = moved(right_used, "blk", left)
    from_left = moved(right_used, "blk", right)
    far_low = moved(from_left[:, :half], "blk", right)
    far_high = moved(from_right[:, half:], "blk", left)

    def left_pair(offset):
        k = (col + offset) % row_len
        own = lax.dynamic_index_in_dim(left_used, row * row_len + k, 1, keepdims=False)
        return jnp.concatenate([own, partner_left[offset]], axis=0)

    def product(lhs, rhs):
        return jnp.einsum("rtxy,tcyz->rcxz", lhs, rhs, precision=highest)

    partial_value = product(left_pair(0), right_used)
    partial_value = partial_value + product(left_pair(1), from_right)
    partial_value = partial_value + product(left_pair(row_len - 1), from_left)
    far = left_pair(2)
    partial_value = partial_value + jnp.concatenate(
        [product(far, far_low), product(far, far_high)], axis=1
    )

    n_hi, n_z, n_core = wide_layout
    hi = me_wide // (n_z * n_core)
    zi = (me_wide // n_core) % n_z
    ci = me_wide % n_core

    def wide_of(h, z, c):
        return (h * n_z + z) * n_core + c

    def sibling(w):
        return wide_of(w // (n_z * n_core), (w // n_core) % n_z, (w % n_core + 1) % n_core)

    def z_next(w):
        return wide_of(w // (n_z * n_core), ((w // n_core) % n_z + 1) % n_z, w % n_core)

    def z_prev(w):
        return wide_of(w // (n_z * n_core), ((w // n_core) % n_z - 1) % n_z, w % n_core)

    def hi_partner(w):
        return wide_of((w // (n_z * n_core) + 1) % n_hi, (w // n_core) % n_z, w % n_core)

    received = moved(partial_value, "wide", sibling)
    block_count = rows_here * cols_here
    slots_each = 2
    owners = wide_of(jnp.arange(n_hi)[:, None], jnp.arange(n_z)[None, :], ci).astype(jnp.int32)

    def selector(owner_list):
        owner_hit = (owner_list[:, None, None] == owners[None]).astype(jnp.int32)
        slot_rank = jnp.cumsum(owner_hit, axis=0) - owner_hit
        slot_match = (slot_rank[..., None] == jnp.arange(slots_each, dtype=jnp.int32)).astype(
            jnp.int32
        )
        return (owner_hit[..., None] * slot_match).astype(jnp.float32)

    chooser = jnp.stack(
        [selector(owner_map.reshape(block_count)), selector(partner_owners.reshape(block_count))]
    ).reshape(2, rows_here, cols_here, n_hi, n_z, slots_each)

    def pick(value):
        value = value.reshape(2, rows_here, cols_here, block_side, block_side)
        return jnp.einsum("puchzs,pucxy->phzsxy", chooser, value, precision=highest)

    acc = pick(partial_value) + pick(received)
    def chunk(value, index):
        return lax.dynamic_index_in_dim(value, index % n_z, 2, keepdims=False)

    forward_steps = (n_z - 1) // 2
    backward_steps = n_z - 1 - forward_steps
    sent_ahead = chunk(acc, zi + forward_steps)
    for step in range(forward_steps):
        got_ahead = moved(sent_ahead, "wide", z_next)
        if step + 1 < forward_steps:
            sent_ahead = got_ahead + chunk(acc, zi + forward_steps - step - 1)
    sent_behind = chunk(acc, zi - backward_steps)
    for step in range(backward_steps):
        got_behind = moved(sent_behind, "wide", z_prev)
        if step + 1 < backward_steps:
            sent_behind = got_behind + chunk(acc, zi - backward_steps + step + 1)
    done_z = chunk(acc, zi) + got_ahead + got_behind
    kept = lax.dynamic_index_in_dim(done_z, hi, 1, keepdims=False)
    given = lax.dynamic_index_in_dim(done_z, (hi + 1) % n_hi, 1, keepdims=False)
    reduced = kept + moved(given, "wide", hi_partner)
    slots = reduced[0] + moved(reduced[1], "blk", partner)
    return slots[None, None]


def solution(mesh):
    in_specs = (
        P("blk", None, "wide", None, None, None),
        P("blk", None, "wide", None),
        P("blk", "wide", None, None, None, None),
        P("blk", "wide", None, None),
        P("blk", None),
    )
    out_specs = P("blk", "wide", None, None, None)
    row_len = 4
    wide_layout = (2, 8, 2)

    def body(*args):
        return per_device(*args, row_len=row_len, wide_layout=wide_layout)

    return jax.shard_map(
        body, mesh=mesh, in_specs=in_specs, out_specs=out_specs, check_vma=False
    )
```

```python
import jax
import jax.numpy as jnp
from jax import lax
from jax.sharding import PartitionSpec as P


def moved(value, axis, target):
    devices = lax.axis_size(axis)
    return lax.ppermute(value, axis, [(i, target(i)) for i in range(devices)])


def per_device(a_blocks, a_map, b_blocks, b_map, owner_map, row_len, wide_layout):
    highest = lax.Precision.HIGHEST
    cycle_size = lax.axis_size("blk")
    wide_size = lax.axis_size("wide")
    n_rows = cycle_size // row_len
    myself = lax.axis_index("blk")
    me_wide = lax.axis_index("wide")
    row = myself // row_len
    col = myself % row_len
    other_row = (row + 1) % n_rows

    def right(i):
        return (i // row_len) * row_len + (i % row_len + 1) % row_len

    def left(i):
        return (i // row_len) * row_len + (i % row_len - 1) % row_len

    def partner(i):
        return (i + row_len) % cycle_size

    left_used = a_blocks[:, :, 0] * a_map[:, :, 0, :, None, None].astype(jnp.float32)
    right_used = b_blocks[0, 0] * b_map[0, 0][:, :, None, None].astype(jnp.float32)
    rows_here, cols_here = owner_map.shape
    block_side = right_used.shape[-1]
    half = cols_here // 2

    partner_left = {}
    for offset in (0, 1, row_len - 1, 2):
        sent = lax.dynamic_index_in_dim(
            left_used, other_row * row_len + (col + offset) % row_len, 1, keepdims=False
        )
        partner_left[offset] = moved(sent, "blk", partner)

    partner_owners = moved(owner_map, "blk", partner)

    from_right = moved(right_used, "blk", left)
    from_left = moved(right_used, "blk", right)
    far_low = moved(from_left[:, :half], "blk", right)
    far_high = moved(from_right[:, half:], "blk", left)

    def left_pair(offset):
        k = (col + offset) % row_len
        own = lax.dynamic_index_in_dim(left_used, row * row_len + k, 1, keepdims=False)
        return jnp.concatenate([own, partner_left[offset]], axis=0)

    def product(lhs, rhs):
        return jnp.einsum("rtxy,tcyz->rcxz", lhs, rhs, precision=highest)

    partial_value = product(left_pair(0), right_used)
    partial_value = partial_value + product(left_pair(1), from_right)
    partial_value = partial_value + product(left_pair(row_len - 1), from_left)
    far = left_pair(2)
    partial_value = partial_value + jnp.concatenate(
        [product(far, far_low), product(far, far_high)], axis=1
    )

    n_hi, n_z, n_core = wide_layout
    hi = me_wide // (n_z * n_core)
    zi = (me_wide // n_core) % n_z
    ci = me_wide % n_core

    def wide_of(h, z, c):
        return (h * n_z + z) * n_core + c

    def sibling(w):
        return wide_of(w // (n_z * n_core), (w // n_core) % n_z, (w % n_core + 1) % n_core)

    def z_next(w):
        return wide_of(w // (n_z * n_core), ((w // n_core) % n_z + 1) % n_z, w % n_core)

    def z_prev(w):
        return wide_of(w // (n_z * n_core), ((w // n_core) % n_z - 1) % n_z, w % n_core)

    def hi_partner(w):
        return wide_of((w // (n_z * n_core) + 1) % n_hi, (w // n_core) % n_z, w % n_core)

    partial_value = partial_value + moved(partial_value, "wide", sibling)
    block_count = rows_here * cols_here
    stacked = partial_value.reshape(2, block_count, block_side, block_side)
    slots_each = 2
    owners = wide_of(jnp.arange(n_hi)[:, None], jnp.arange(n_z)[None, :], ci).astype(jnp.int32)

    def selector(owner_list):
        owner_hit = (owner_list[:, None, None] == owners[None]).astype(jnp.int32)
        slot_rank = jnp.cumsum(owner_hit, axis=0) - owner_hit
        slot_match = (slot_rank[..., None] == jnp.arange(slots_each, dtype=jnp.int32)).astype(
            jnp.int32
        )
        return (owner_hit[..., None] * slot_match).astype(jnp.float32)

    chooser = jnp.stack(
        [selector(owner_map.reshape(block_count)), selector(partner_owners.reshape(block_count))]
    )
    acc = jnp.einsum("pqhzs,pqxy->phzsxy", chooser, stacked, precision=highest)
    def chunk(value, index):
        return lax.dynamic_index_in_dim(value, index % n_z, 2, keepdims=False)

    steps = n_z // 2
    sent_ahead = chunk(acc, zi + steps)[:, :, 0]
    sent_behind = chunk(acc, zi - steps)[:, :, 1]
    for step in range(steps):
        got_ahead = moved(sent_ahead, "wide", z_next)
        got_behind = moved(sent_behind, "wide", z_prev)
        if step + 1 < steps:
            next_ahead = chunk(acc, zi + steps - step - 1)
            next_behind = chunk(acc, zi - steps + step + 1)
            if step == 0:
                sent_ahead = next_ahead.at[:, :, 0].add(got_ahead)
                sent_behind = next_behind.at[:, :, 1].add(got_behind)
            else:
                sent_ahead = next_ahead + got_ahead
                sent_behind = next_behind + got_behind
    done_z = chunk(acc, zi) + got_ahead + got_behind
    there = (hi + 1) % n_hi
    own_here = done_z[0, hi]
    from_hi = moved(done_z[0, there], "wide", hi_partner)
    from_partner = moved(done_z[1, hi], "blk", partner)
    across = lax.ppermute(
        done_z[1, there],
        ("blk", "wide"),
        [
            (b * wide_size + w, partner(b) * wide_size + hi_partner(w))
            for b in range(cycle_size)
            for w in range(wide_size)
        ],
    )
    slots = own_here + from_hi + from_partner + across
    return slots[None, None]


def solution(mesh):
    in_specs = (
        P("blk", None, "wide", None, None, None),
        P("blk", None, "wide", None),
        P("blk", "wide", None, None, None, None),
        P("blk", "wide", None, None),
        P("blk", None),
    )
    out_specs = P("blk", "wide", None, None, None)
    row_len = 4
    wide_layout = (2, 8, 2)

    def body(*args):
        return per_device(*args, row_len=row_len, wide_layout=wide_layout)

    return jax.shard_map(
        body, mesh=mesh, in_specs=in_specs, out_specs=out_specs, check_vma=False
    )
```

```python
import jax
import jax.numpy as jnp
from jax import lax
from jax.sharding import PartitionSpec as P


def moved(value, axis, target):
    devices = lax.axis_size(axis)
    return lax.ppermute(value, axis, [(i, target(i)) for i in range(devices)])


def per_device(a_blocks, a_map, b_blocks, b_map, owner_map, row_len, wide_layout):
    highest = lax.Precision.HIGHEST
    cycle_size = lax.axis_size("blk")
    wide_size = lax.axis_size("wide")
    n_rows = cycle_size // row_len
    myself = lax.axis_index("blk")
    me_wide = lax.axis_index("wide")
    row = myself // row_len
    col = myself % row_len
    other_row = (row + 1) % n_rows

    def right(i):
        return (i // row_len) * row_len + (i % row_len + 1) % row_len

    def left(i):
        return (i // row_len) * row_len + (i % row_len - 1) % row_len

    def partner(i):
        return (i + row_len) % cycle_size

    left_used = a_blocks[:, :, 0] * a_map[:, :, 0, :, None, None].astype(jnp.float32)
    right_used = b_blocks[0, 0] * b_map[0, 0][:, :, None, None].astype(jnp.float32)
    rows_here, cols_here = owner_map.shape
    block_side = right_used.shape[-1]
    half = cols_here // 2

    partner_left = {}
    for offset in (0, 1, row_len - 1, 2):
        sent = lax.dynamic_index_in_dim(
            left_used, other_row * row_len + (col + offset) % row_len, 1, keepdims=False
        )
        partner_left[offset] = moved(sent, "blk", partner)

    partner_owners = moved(owner_map, "blk", partner)

    from_right = moved(right_used, "blk", left)
    from_left = moved(right_used, "blk", right)
    far_low = moved(from_left[:, :half], "blk", right)
    far_high = moved(from_right[:, half:], "blk", left)

    def own_left(offset):
        k = (col + offset) % row_len
        return lax.dynamic_index_in_dim(left_used, row * row_len + k, 1, keepdims=False)

    def product(lhs, rhs):
        return jnp.einsum("rtxy,tcyz->rcxz", lhs, rhs, precision=highest)

    def panel_partial(left_of):
        total = product(left_of(0), right_used)
        total = total + product(left_of(1), from_right)
        total = total + product(left_of(row_len - 1), from_left)
        far = left_of(2)
        return total + jnp.concatenate([product(far, far_low), product(far, far_high)], axis=1)

    own_partial = panel_partial(own_left)
    partner_partial = panel_partial(lambda offset: partner_left[offset])

    n_hi, n_z, n_core = wide_layout
    hi = me_wide // (n_z * n_core)
    zi = (me_wide // n_core) % n_z
    ci = me_wide % n_core

    def wide_of(h, z, c):
        return (h * n_z + z) * n_core + c

    def sibling(w):
        return wide_of(w // (n_z * n_core), (w // n_core) % n_z, (w % n_core + 1) % n_core)

    def z_next(w):
        return wide_of(w // (n_z * n_core), ((w // n_core) % n_z + 1) % n_z, w % n_core)

    def z_prev(w):
        return wide_of(w // (n_z * n_core), ((w // n_core) % n_z - 1) % n_z, w % n_core)

    def hi_partner(w):
        return wide_of((w // (n_z * n_core) + 1) % n_hi, (w // n_core) % n_z, w % n_core)

    block_count = rows_here * cols_here
    slots_each = 2
    owners = wide_of(jnp.arange(n_hi)[:, None], jnp.arange(n_z)[None, :], ci).astype(jnp.int32)

    def selector(owner_list):
        owner_hit = (owner_list[:, None, None] == owners[None]).astype(jnp.int32)
        slot_rank = jnp.cumsum(owner_hit, axis=0) - owner_hit
        slot_match = (slot_rank[..., None] == jnp.arange(slots_each, dtype=jnp.int32)).astype(
            jnp.int32
        )
        return (owner_hit[..., None] * slot_match).astype(jnp.float32)

    def core_slots(partial, owner_list):
        summed = partial + moved(partial, "wide", sibling)
        summed = summed.reshape(block_count, block_side, block_side)
        return jnp.einsum("qhzs,qxy->hzsxy", selector(owner_list), summed, precision=highest)

    accs = (
        core_slots(own_partial, owner_map.reshape(block_count)),
        core_slots(partner_partial, partner_owners.reshape(block_count)),
    )
    def chunk(value, index):
        return jnp.stack(
            [lax.dynamic_index_in_dim(part, index % n_z, 1, keepdims=False) for part in value]
        )

    steps = n_z // 2
    sent_ahead = chunk(accs, zi + steps)[:, :, 0]
    sent_behind = chunk(accs, zi - steps)[:, :, 1]
    for step in range(steps):
        got_ahead = moved(sent_ahead, "wide", z_next)
        got_behind = moved(sent_behind, "wide", z_prev)
        if step + 1 < steps:
            next_ahead = chunk(accs, zi + steps - step - 1)
            next_behind = chunk(accs, zi - steps + step + 1)
            if step == 0:
                sent_ahead = next_ahead.at[:, :, 0].add(got_ahead)
                sent_behind = next_behind.at[:, :, 1].add(got_behind)
            else:
                sent_ahead = next_ahead + got_ahead
                sent_behind = next_behind + got_behind
    done_z = chunk(accs, zi) + got_ahead + got_behind
    there = (hi + 1) % n_hi
    own_here = done_z[0, hi]
    from_hi = moved(done_z[0, there], "wide", hi_partner)
    from_partner = moved(done_z[1, hi], "blk", partner)
    across = lax.ppermute(
        done_z[1, there],
        ("blk", "wide"),
        [
            (b * wide_size + w, partner(b) * wide_size + hi_partner(w))
            for b in range(cycle_size)
            for w in range(wide_size)
        ],
    )
    slots = own_here + from_hi + from_partner + across
    return slots[None, None]


def solution(mesh):
    in_specs = (
        P("blk", None, "wide", None, None, None),
        P("blk", None, "wide", None),
        P("blk", "wide", None, None, None, None),
        P("blk", "wide", None, None),
        P("blk", None),
    )
    out_specs = P("blk", "wide", None, None, None)
    row_len = 4
    wide_layout = (2, 8, 2)

    def body(*args):
        return per_device(*args, row_len=row_len, wide_layout=wide_layout)

    return jax.shard_map(
        body, mesh=mesh, in_specs=in_specs, out_specs=out_specs, check_vma=False
    )
```

```python
import jax
import jax.numpy as jnp
from jax import lax
from jax.sharding import PartitionSpec as P


def moved(value, axis, target):
    devices = lax.axis_size(axis)
    return lax.ppermute(value, axis, [(i, target(i)) for i in range(devices)])


def per_device(a_blocks, a_map, b_blocks, b_map, owner_map, row_len, wide_layout):
    highest = lax.Precision.HIGHEST
    cycle_size = lax.axis_size("blk")
    wide_size = lax.axis_size("wide")
    n_rows = cycle_size // row_len
    myself = lax.axis_index("blk")
    me_wide = lax.axis_index("wide")
    row = myself // row_len
    col = myself % row_len
    other_row = (row + 1) % n_rows

    def right(i):
        return (i // row_len) * row_len + (i % row_len + 1) % row_len

    def left(i):
        return (i // row_len) * row_len + (i % row_len - 1) % row_len

    def partner(i):
        return (i + row_len) % cycle_size

    left_used = a_blocks[:, :, 0] * a_map[:, :, 0, :, None, None].astype(jnp.float32)
    right_used = b_blocks[0, 0] * b_map[0, 0][:, :, None, None].astype(jnp.float32)
    rows_here, cols_here = owner_map.shape
    block_side = right_used.shape[-1]
    half = cols_here // 2

    partner_left = {}
    for offset in (0, 1, row_len - 1, 2):
        inner = other_row * row_len + (col + offset) % row_len
        sent = lax.dynamic_index_in_dim(a_blocks[:, :, 0], inner, 1, keepdims=False)
        sent_map = lax.dynamic_index_in_dim(a_map[:, :, 0], inner, 1, keepdims=False)
        partner_left[offset] = moved(sent, "blk", partner) * moved(sent_map, "blk", partner)[
            :, :, None, None
        ].astype(jnp.float32)

    partner_owners = moved(owner_map, "blk", partner)

    from_right = moved(right_used, "blk", left)
    from_left = moved(right_used, "blk", right)
    far_low = moved(from_left[:, :half], "blk", right)
    far_high = moved(from_right[:, half:], "blk", left)

    def left_pair(offset):
        k = (col + offset) % row_len
        own = lax.dynamic_index_in_dim(left_used, row * row_len + k, 1, keepdims=False)
        return jnp.concatenate([own, partner_left[offset]], axis=0)

    def product(lhs, rhs):
        return jnp.einsum("rtxy,tcyz->rcxz", lhs, rhs, precision=highest)

    partial_value = product(left_pair(0), right_used)
    partial_value = partial_value + product(left_pair(1), from_right)
    partial_value = partial_value + product(left_pair(row_len - 1), from_left)
    far = left_pair(2)
    partial_value = partial_value + jnp.concatenate(
        [product(far, far_low), product(far, far_high)], axis=1
    )

    n_hi, n_z, n_core = wide_layout
    hi = me_wide // (n_z * n_core)
    zi = (me_wide // n_core) % n_z
    ci = me_wide % n_core

    def wide_of(h, z, c):
        return (h * n_z + z) * n_core + c

    def sibling(w):
        return wide_of(w // (n_z * n_core), (w // n_core) % n_z, (w % n_core + 1) % n_core)

    def z_next(w):
        return wide_of(w // (n_z * n_core), ((w // n_core) % n_z + 1) % n_z, w % n_core)

    def z_prev(w):
        return wide_of(w // (n_z * n_core), ((w // n_core) % n_z - 1) % n_z, w % n_core)

    def hi_partner(w):
        return wide_of((w // (n_z * n_core) + 1) % n_hi, (w // n_core) % n_z, w % n_core)

    partial_value = partial_value + moved(partial_value, "wide", sibling)
    block_count = rows_here * cols_here
    stacked = partial_value.reshape(2, block_count, block_side, block_side)
    slots_each = 2
    owners = wide_of(jnp.arange(n_hi)[:, None], jnp.arange(n_z)[None, :], ci).astype(jnp.int32)

    def selector(owner_list):
        owner_hit = (owner_list[:, None, None] == owners[None]).astype(jnp.int32)
        slot_rank = jnp.cumsum(owner_hit, axis=0) - owner_hit
        slot_match = (slot_rank[..., None] == jnp.arange(slots_each, dtype=jnp.int32)).astype(
            jnp.int32
        )
        return (owner_hit[..., None] * slot_match).astype(jnp.float32)

    chooser = jnp.stack(
        [selector(owner_map.reshape(block_count)), selector(partner_owners.reshape(block_count))]
    )
    acc = jnp.einsum("pqhzs,pqxy->phzsxy", chooser, stacked, precision=highest)
    def chunk(value, index):
        return lax.dynamic_index_in_dim(value, index % n_z, 2, keepdims=False)

    steps = n_z // 2
    sent_ahead = chunk(acc, zi + steps)[:, :, 0]
    sent_behind = chunk(acc, zi - steps)[:, :, 1]
    for step in range(steps):
        got_ahead = moved(sent_ahead, "wide", z_next)
        got_behind = moved(sent_behind, "wide", z_prev)
        if step + 1 < steps:
            next_ahead = chunk(acc, zi + steps - step - 1)
            next_behind = chunk(acc, zi - steps + step + 1)
            if step == 0:
                sent_ahead = next_ahead.at[:, :, 0].add(got_ahead)
                sent_behind = next_behind.at[:, :, 1].add(got_behind)
            else:
                sent_ahead = next_ahead + got_ahead
                sent_behind = next_behind + got_behind
    done_z = chunk(acc, zi) + got_ahead + got_behind
    there = (hi + 1) % n_hi
    own_here = done_z[0, hi]
    from_hi = moved(done_z[0, there], "wide", hi_partner)
    from_partner = moved(done_z[1, hi], "blk", partner)
    across = lax.ppermute(
        done_z[1, there],
        ("blk", "wide"),
        [
            (b * wide_size + w, partner(b) * wide_size + hi_partner(w))
            for b in range(cycle_size)
            for w in range(wide_size)
        ],
    )
    slots = own_here + from_hi + from_partner + across
    return slots[None, None]


def solution(mesh):
    in_specs = (
        P("blk", None, "wide", None, None, None),
        P("blk", None, "wide", None),
        P("blk", "wide", None, None, None, None),
        P("blk", "wide", None, None),
        P("blk", None),
    )
    out_specs = P("blk", "wide", None, None, None)
    row_len = 4
    wide_layout = (2, 8, 2)

    def body(*args):
        return per_device(*args, row_len=row_len, wide_layout=wide_layout)

    return jax.shard_map(
        body, mesh=mesh, in_specs=in_specs, out_specs=out_specs, check_vma=False
    )
```

```python
import jax
import jax.numpy as jnp
from jax import lax
from jax.sharding import PartitionSpec as P


def moved(value, axis, target):
    devices = lax.axis_size(axis)
    return lax.ppermute(value, axis, [(i, target(i)) for i in range(devices)])


def per_device(a_blocks, a_map, b_blocks, b_map, owner_map, row_len, wide_layout):
    highest = lax.Precision.HIGHEST
    cycle_size = lax.axis_size("blk")
    wide_size = lax.axis_size("wide")
    n_rows = cycle_size // row_len
    myself = lax.axis_index("blk")
    me_wide = lax.axis_index("wide")
    row = myself // row_len
    col = myself % row_len
    other_row = (row + 1) % n_rows

    def right(i):
        return (i // row_len) * row_len + (i % row_len + 1) % row_len

    def left(i):
        return (i // row_len) * row_len + (i % row_len - 1) % row_len

    def partner(i):
        return (i + row_len) % cycle_size

    left_used = a_blocks[:, :, 0] * a_map[:, :, 0, :, None, None].astype(jnp.float32)
    right_used = b_blocks[0, 0] * b_map[0, 0][:, :, None, None].astype(jnp.float32)
    rows_here, cols_here = owner_map.shape
    block_side = right_used.shape[-1]
    half = cols_here // 2

    partner_left = {}
    for offset in (0, 1, row_len - 1, 2):
        sent = lax.dynamic_index_in_dim(
            left_used, other_row * row_len + (col + offset) % row_len, 1, keepdims=False
        )
        partner_left[offset] = moved(sent, "blk", partner)

    partner_owners = moved(owner_map, "blk", partner)

    from_right = moved(right_used, "blk", left)
    from_left = moved(right_used, "blk", right)
    far_low = moved(from_left[:, :half], "blk", right)
    far_high = moved(from_right[:, half:], "blk", left)

    def left_pair(offset):
        k = (col + offset) % row_len
        own = lax.dynamic_index_in_dim(left_used, row * row_len + k, 1, keepdims=False)
        return jnp.concatenate([own, partner_left[offset]], axis=0)

    def product(lhs, rhs):
        return jnp.einsum("rtxy,tcyz->rcxz", lhs, rhs, precision=lax.Precision.HIGH)

    partial_value = product(left_pair(0), right_used)
    partial_value = partial_value + product(left_pair(1), from_right)
    partial_value = partial_value + product(left_pair(row_len - 1), from_left)
    far = left_pair(2)
    partial_value = partial_value + jnp.concatenate(
        [product(far, far_low), product(far, far_high)], axis=1
    )

    n_hi, n_z, n_core = wide_layout
    hi = me_wide // (n_z * n_core)
    zi = (me_wide // n_core) % n_z
    ci = me_wide % n_core

    def wide_of(h, z, c):
        return (h * n_z + z) * n_core + c

    def sibling(w):
        return wide_of(w // (n_z * n_core), (w // n_core) % n_z, (w % n_core + 1) % n_core)

    def z_next(w):
        return wide_of(w // (n_z * n_core), ((w // n_core) % n_z + 1) % n_z, w % n_core)

    def z_prev(w):
        return wide_of(w // (n_z * n_core), ((w // n_core) % n_z - 1) % n_z, w % n_core)

    def hi_partner(w):
        return wide_of((w // (n_z * n_core) + 1) % n_hi, (w // n_core) % n_z, w % n_core)

    partial_value = partial_value + moved(partial_value, "wide", sibling)
    block_count = rows_here * cols_here
    stacked = partial_value.reshape(2, block_count, block_side, block_side)
    slots_each = 2
    owners = wide_of(jnp.arange(n_hi)[:, None], jnp.arange(n_z)[None, :], ci).astype(jnp.int32)

    def selector(owner_list):
        owner_hit = (owner_list[:, None, None] == owners[None]).astype(jnp.int32)
        slot_rank = jnp.cumsum(owner_hit, axis=0) - owner_hit
        slot_match = (slot_rank[..., None] == jnp.arange(slots_each, dtype=jnp.int32)).astype(
            jnp.int32
        )
        return (owner_hit[..., None] * slot_match).astype(jnp.float32)

    chooser = jnp.stack(
        [selector(owner_map.reshape(block_count)), selector(partner_owners.reshape(block_count))]
    )
    acc = jnp.einsum("pqhzs,pqxy->phzsxy", chooser, stacked, precision=highest)
    def chunk(value, index):
        return lax.dynamic_index_in_dim(value, index % n_z, 2, keepdims=False)

    steps = n_z // 2
    sent_ahead = chunk(acc, zi + steps)[:, :, 0]
    sent_behind = chunk(acc, zi - steps)[:, :, 1]
    for step in range(steps):
        got_ahead = moved(sent_ahead, "wide", z_next)
        got_behind = moved(sent_behind, "wide", z_prev)
        if step + 1 < steps:
            next_ahead = chunk(acc, zi + steps - step - 1)
            next_behind = chunk(acc, zi - steps + step + 1)
            if step == 0:
                sent_ahead = next_ahead.at[:, :, 0].add(got_ahead)
                sent_behind = next_behind.at[:, :, 1].add(got_behind)
            else:
                sent_ahead = next_ahead + got_ahead
                sent_behind = next_behind + got_behind
    done_z = chunk(acc, zi) + got_ahead + got_behind
    there = (hi + 1) % n_hi
    own_here = done_z[0, hi]
    from_hi = moved(done_z[0, there], "wide", hi_partner)
    from_partner = moved(done_z[1, hi], "blk", partner)
    across = lax.ppermute(
        done_z[1, there],
        ("blk", "wide"),
        [
            (b * wide_size + w, partner(b) * wide_size + hi_partner(w))
            for b in range(cycle_size)
            for w in range(wide_size)
        ],
    )
    slots = own_here + from_hi + from_partner + across
    return slots[None, None]


def solution(mesh):
    in_specs = (
        P("blk", None, "wide", None, None, None),
        P("blk", None, "wide", None),
        P("blk", "wide", None, None, None, None),
        P("blk", "wide", None, None),
        P("blk", None),
    )
    out_specs = P("blk", "wide", None, None, None)
    row_len = 4
    wide_layout = (2, 8, 2)

    def body(*args):
        return per_device(*args, row_len=row_len, wide_layout=wide_layout)

    return jax.shard_map(
        body, mesh=mesh, in_specs=in_specs, out_specs=out_specs, check_vma=False
    )
```

```python
import jax
import jax.numpy as jnp
from jax import lax
from jax.sharding import PartitionSpec as P


def moved(value, axis, target):
    devices = lax.axis_size(axis)
    return lax.ppermute(value, axis, [(i, target(i)) for i in range(devices)])


def per_device(a_blocks, a_map, b_blocks, b_map, owner_map, row_len, wide_layout):
    highest = lax.Precision.HIGHEST
    cycle_size = lax.axis_size("blk")
    wide_size = lax.axis_size("wide")
    n_rows = cycle_size // row_len
    myself = lax.axis_index("blk")
    me_wide = lax.axis_index("wide")
    row = myself // row_len
    col = myself % row_len
    other_row = (row + 1) % n_rows

    def right(i):
        return (i // row_len) * row_len + (i % row_len + 1) % row_len

    def left(i):
        return (i // row_len) * row_len + (i % row_len - 1) % row_len

    def partner(i):
        return (i + row_len) % cycle_size

    left_used = a_blocks[:, :, 0] * a_map[:, :, 0, :, None, None].astype(jnp.float32)
    right_used = b_blocks[0, 0] * b_map[0, 0][:, :, None, None].astype(jnp.float32)
    rows_here, cols_here = owner_map.shape
    block_side = right_used.shape[-1]
    half = cols_here // 2

    partner_left = {}
    for offset in (0, 1, row_len - 1, 2):
        sent = lax.dynamic_index_in_dim(
            left_used, other_row * row_len + (col + offset) % row_len, 1, keepdims=False
        )
        partner_left[offset] = moved(sent, "blk", partner)

    partner_owners = moved(owner_map, "blk", partner)

    from_right = moved(right_used, "blk", left)
    from_left = moved(right_used, "blk", right)
    far_low = moved(from_left[:, :half], "blk", right)
    far_high = moved(from_right[:, half:], "blk", left)

    def left_pair(offset):
        k = (col + offset) % row_len
        own = lax.dynamic_index_in_dim(left_used, row * row_len + k, 1, keepdims=False)
        return jnp.concatenate([own, partner_left[offset]], axis=0)

    def product(lhs, rhs):
        return jnp.einsum("rtxy,tcyz->rcxz", lhs, rhs, precision=lax.Precision.HIGH)

    partial_value = product(left_pair(0), right_used)
    partial_value = partial_value + product(left_pair(1), from_right)
    partial_value = partial_value + product(left_pair(row_len - 1), from_left)
    far = left_pair(2)
    partial_value = partial_value + jnp.concatenate(
        [product(far, far_low), product(far, far_high)], axis=1
    )

    n_hi, n_z, n_core = wide_layout
    hi = me_wide // (n_z * n_core)
    zi = (me_wide // n_core) % n_z
    ci = me_wide % n_core

    def wide_of(h, z, c):
        return (h * n_z + z) * n_core + c

    def sibling(w):
        return wide_of(w // (n_z * n_core), (w // n_core) % n_z, (w % n_core + 1) % n_core)

    def z_next(w):
        return wide_of(w // (n_z * n_core), ((w // n_core) % n_z + 1) % n_z, w % n_core)

    def z_prev(w):
        return wide_of(w // (n_z * n_core), ((w // n_core) % n_z - 1) % n_z, w % n_core)

    def hi_partner(w):
        return wide_of((w // (n_z * n_core) + 1) % n_hi, (w // n_core) % n_z, w % n_core)

    partial_value = partial_value + moved(partial_value, "wide", sibling)
    block_count = rows_here * cols_here
    stacked = partial_value.reshape(2, block_count, block_side, block_side)
    slots_each = 2
    owners = wide_of(jnp.arange(n_hi)[:, None], jnp.arange(n_z)[None, :], ci).astype(jnp.int32)

    def selector(owner_list):
        owner_hit = (owner_list[:, None, None] == owners[None]).astype(jnp.int32)
        slot_rank = jnp.cumsum(owner_hit, axis=0) - owner_hit
        slot_match = (slot_rank[..., None] == jnp.arange(slots_each, dtype=jnp.int32)).astype(
            jnp.int32
        )
        return (owner_hit[..., None] * slot_match).astype(jnp.float32)

    chooser = jnp.stack(
        [selector(owner_map.reshape(block_count)), selector(partner_owners.reshape(block_count))]
    )
    acc = jnp.einsum("pqhzs,pqxy->phzsxy", chooser, stacked, precision=lax.Precision.HIGH)
    def chunk(value, index):
        return lax.dynamic_index_in_dim(value, index % n_z, 2, keepdims=False)

    steps = n_z // 2
    sent_ahead = chunk(acc, zi + steps)[:, :, 0]
    sent_behind = chunk(acc, zi - steps)[:, :, 1]
    for step in range(steps):
        got_ahead = moved(sent_ahead, "wide", z_next)
        got_behind = moved(sent_behind, "wide", z_prev)
        if step + 1 < steps:
            next_ahead = chunk(acc, zi + steps - step - 1)
            next_behind = chunk(acc, zi - steps + step + 1)
            if step == 0:
                sent_ahead = next_ahead.at[:, :, 0].add(got_ahead)
                sent_behind = next_behind.at[:, :, 1].add(got_behind)
            else:
                sent_ahead = next_ahead + got_ahead
                sent_behind = next_behind + got_behind
    done_z = chunk(acc, zi) + got_ahead + got_behind
    there = (hi + 1) % n_hi
    own_here = done_z[0, hi]
    from_hi = moved(done_z[0, there], "wide", hi_partner)
    from_partner = moved(done_z[1, hi], "blk", partner)
    across = lax.ppermute(
        done_z[1, there],
        ("blk", "wide"),
        [
            (b * wide_size + w, partner(b) * wide_size + hi_partner(w))
            for b in range(cycle_size)
            for w in range(wide_size)
        ],
    )
    slots = own_here + from_hi + from_partner + across
    return slots[None, None]


def solution(mesh):
    in_specs = (
        P("blk", None, "wide", None, None, None),
        P("blk", None, "wide", None),
        P("blk", "wide", None, None, None, None),
        P("blk", "wide", None, None),
        P("blk", None),
    )
    out_specs = P("blk", "wide", None, None, None)
    row_len = 4
    wide_layout = (2, 8, 2)

    def body(*args):
        return per_device(*args, row_len=row_len, wide_layout=wide_layout)

    return jax.shard_map(
        body, mesh=mesh, in_specs=in_specs, out_specs=out_specs, check_vma=False
    )
```
